256 devices in a mesh: row: 8 (over z), col: 32 (over y, x, core).
Axes of the slice: x: 4, y: 4, z: 8, core: 2. Of those that a mesh axis runs over, the one named last changes fastest.
Arguments:
- kernel: float32 [8, 8, 256, 2, 32, 256], P(None, 'row', None, None, 'col'), may hold values from 0 to 1.3, as said below
Outputs:
- factored: float32 [8, 8, 256, 2, 32, 256], P(None, 'row', None, None, 'col')
The draws below stay inside these ranges and needn't reach their ends.
Inputs may be any that keep to these rules, and one draw needn't show every extreme that they name: kernel is symmetric and positive definite.
All inputs are finite; a program needn't handle non-finite values.
Results may differ from the reference program's by a relative error of at most 0.0003.
Values sent between devices are 32-bit elements; how exact they have to be, the bound alone decides.
No kernel may reach another device: no remote copies, remote signals or barrier semaphores. Data moves between devices by JAX's collectives and lax.ppermute only.
A program may use at most 64 MiB of HBM per device.

```python
import jax
import jax.numpy as jnp
from jax import lax

NB = 256
M = 16384
PANELS = 2
TR_DEV = 8
TC_DEV = 2
N_ROW = 8
N_COL = 32


def draw_kernel(key, part):
    first = jax.random.fold_in(key, 11)
    second = jax.random.fold_in(key, 12)
    third = jax.random.fold_in(key, 13)
    hurst = jax.random.uniform(third, (), jnp.float32, 0.07, 0.15)
    times = jax.random.uniform(first, (M,), jnp.float32, 0.01, 1.0)
    power = 2.0 * hurst
    marginal = jnp.power(times, power)
    spacing = jnp.abs(times[:, None] - times[None, :])
    covariance = 0.5 * (marginal[:, None] + marginal[None, :] - jnp.power(spacing, power))
    nugget = jax.random.uniform(second, (M,), jnp.float32, 0.1, 0.3)
    index = jnp.arange(M)
    covariance = covariance.at[index, index].add(nugget)
    return covariance.reshape(TR_DEV, N_ROW, NB, TC_DEV, N_COL, NB)


def setup_inputs(seed: int = 0) -> dict:
    keys = jax.random.split(jax.random.key(seed), 2)
    kernel = draw_kernel(jax.random.fold_in(keys[1], 71), 0)
    return {"kernel": kernel}


def reference(kernel):
    whole = kernel.reshape(M, M)
    for k in range(PANELS):
        start = k * NB
        column = whole[:, start:start + NB]
        lower = jnp.linalg.cholesky(column[start:start + NB])
        panel = jax.scipy.linalg.solve_triangular(lower, column.T, lower=True).T
        panel = panel.at[start:start + NB].set(lower)
        panel = panel.at[:start].set(jnp.zeros((start, NB), jnp.float32))
        after = start + NB
        update = jnp.dot(panel.astype(jnp.float32), panel[after:].T.astype(jnp.float32), precision=lax.Precision.HIGHEST, preferred_element_type=jnp.float32)
        whole = whole.at[:, after:].add(-update)
        whole = whole.at[:, start:start + NB].set(panel)
    edge = PANELS * NB
    whole = whole.at[:edge, edge:].set(jnp.zeros((edge, M - edge), jnp.float32))
    return whole.reshape(TR_DEV, N_ROW, NB, TC_DEV, N_COL, NB)
```

```python
import jax
import jax.numpy as jnp
from jax import lax
from jax.sharding import PartitionSpec as P

HIGH = lax.Precision.HIGHEST


def prescatter(pieces, axis, plan):
    me = lax.axis_index(axis)
    got = jnp.zeros_like(pieces[0])
    for q, pairs in enumerate(plan):
        moved = [(s, d) for s, d in pairs if s != d]
        kept = [s for s, d in pairs if s == d]
        if moved:
            got = got + lax.ppermute(pieces[q], axis, moved)
        for s in kept:
            got = got + jnp.where(me == s, pieces[q], jnp.zeros_like(pieces[q]))
    return got


def tri_solve(lower, rows):
    n, w = rows.shape[0], rows.shape[1]
    flat = rows.reshape(n * w, w)
    return jax.scipy.linalg.solve_triangular(lower, flat.T, lower=True).T.reshape(n, w, w)


def per_device(kernel):
    tiles, width, ucount = kernel.shape[0], kernel.shape[2], kernel.shape[3]
    work = kernel.reshape(tiles, width, ucount, width)
    nrow = lax.axis_size("row")
    ncol = lax.axis_size("col")
    my_row = lax.axis_index("row")
    my_col = lax.axis_index("col")
    half = width // 2

    rowblk = work[0]
    cpieces = [rowblk[(p % 2) * half:(p % 2 + 1) * half, p // 2, :] for p in range(2 * ucount)]
    d0 = [(-p) % nrow for p in range(2 * ucount)]
    d1 = [(1 + p) % nrow for p in range(2 * ucount)]
    cplan = [[(0, d0[p]), (1, d1[p])] for p in range(2 * ucount)]
    cmine = prescatter(cpieces, "row", cplan)
    cg = lax.all_gather(cmine, "row")

    def cblock(dest, u):
        return jnp.concatenate([cg[dest[2 * u]], cg[dest[2 * u + 1]]], axis=0)

    crow = [[cblock(d, u) for u in range(ucount)] for d in (d0, d1)]

    lead = jnp.concatenate([crow[0][0], crow[1][0]], axis=0)
    pcol = work[:, :, 0, :].reshape(tiles * width, width)
    npieces = ncol // 2
    rrows = pcol.shape[0] // npieces
    lrows = lead.shape[0] // npieces
    rplan = [[(0, 2 * q), (1, 2 * q + 1)] for q in range(npieces)]
    rmine = prescatter([pcol[q * rrows:(q + 1) * rrows] for q in range(npieces)], "col", rplan)
    lmine = prescatter([lead[q * lrows:(q + 1) * lrows] for q in range(npieces)], "col", rplan)
    rg = lax.all_gather(jnp.concatenate([rmine, lmine], axis=0), "col")

    def assemble(k):
        body = jnp.concatenate([rg[2 * q + k, :rrows] for q in range(npieces)], axis=0)
        tail = jnp.concatenate([rg[2 * q + k, rrows:] for q in range(npieces)], axis=0)
        return body.reshape(tiles, width, width), tail

    col0, lead0 = assemble(0)
    col1, lead1 = assemble(1)
    a00 = lead0[:width]
    a10 = lead0[width:]
    a11 = lead1[width:]

    block_rows = jnp.arange(tiles, dtype=jnp.int32) * nrow + my_row
    block_cols = jnp.arange(ucount, dtype=jnp.int32) * ncol + my_col
    cT0 = jnp.stack([crow[0][u].T for u in range(ucount)])
    cT1 = jnp.stack([crow[1][u].T for u in range(ucount)])

    g0 = jnp.linalg.cholesky(a00)
    x0 = tri_solve(g0, jnp.concatenate([col0, cT0, a10[None]], axis=0))
    x0r, x0c, x01 = x0[:tiles], x0[tiles:tiles + ucount], x0[tiles + ucount]
    a11u = a11 - jnp.dot(x01, x01.T, precision=HIGH, preferred_element_type=jnp.float32)
    g1 = jnp.linalg.cholesky(a11u)
    y1 = jnp.concatenate([col1, cT1], axis=0) - jnp.einsum(
        "nab,cb->nac", jnp.concatenate([x0r, x0c], axis=0), x01,
        precision=HIGH, preferred_element_type=jnp.float32)
    x1 = tri_solve(g1, y1)
    x1r, x1c = x1[:tiles], x1[tiles:]

    def mask(x, idx, k, g):
        later = (idx > k)[:, None, None]
        same = (idx == k)[:, None, None]
        return jnp.where(later, x, jnp.where(same, g[None], 0.0))

    p0r = mask(x0r, block_rows, 0, g0)
    p0c = mask(x0c, block_cols, 0, g0)
    p1r = mask(x1r, block_rows, 1, g1)
    p1c = mask(x1c, block_cols, 1, g1)

    def update(w, k, pr, pc):
        prod = jnp.einsum("iab,jcb->iajc", pr, pc, precision=HIGH,
                          preferred_element_type=jnp.float32)
        later = (block_cols > k)[None, None, :, None]
        same = (block_cols == k)[None, None, :, None]
        w = jnp.where(later, w - prod, w)
        return jnp.where(same, pr[:, :, None, :], w)

    work = update(work, 0, p0r, p0c)
    work = update(work, 1, p1r, p1c)
    upper = (block_rows < 2)[:, None, None, None] & (block_cols >= 2)[None, None, :, None]
    work = jnp.where(upper, 0.0, work)
    return work.reshape(tiles, 1, width, ucount, 1, width)


def solution(mesh):
    in_specs = (P(None, "row", None, None, "col", None),)
    out_specs = P(None, "row", None, None, "col", None)
    return jax.shard_map(
        per_device, mesh=mesh, in_specs=in_specs, out_specs=out_specs, check_vma=False
    )
```

```python
import jax
import jax.numpy as jnp
from jax import lax
from jax.sharding import PartitionSpec as P

HIGH = lax.Precision.HIGHEST


def prescatter(pieces, axis, plan):
    me = lax.axis_index(axis)
    got = jnp.zeros_like(pieces[0])
    for q, pairs in enumerate(plan):
        moved = [(s, d) for s, d in pairs if s != d]
        kept = [s for s, d in pairs if s == d]
        if moved:
            got = got + lax.ppermute(pieces[q], axis, moved)
        for s in kept:
            got = got + jnp.where(me == s, pieces[q], jnp.zeros_like(pieces[q]))
    return got


def per_device(kernel):
    tiles, width, ucount = kernel.shape[0], kernel.shape[2], kernel.shape[3]
    work = kernel.reshape(tiles, width, ucount, width)
    nrow = lax.axis_size("row")
    ncol = lax.axis_size("col")
    my_row = lax.axis_index("row")
    my_col = lax.axis_index("col")
    half = width // 2

    rowblk = work[0]
    cpieces = [rowblk[(p % 2) * half:(p % 2 + 1) * half, p // 2, :] for p in range(2 * ucount)]
    d0 = [(-p) % nrow for p in range(2 * ucount)]
    d1 = [(1 + p) % nrow for p in range(2 * ucount)]
    cplan = [[(0, d0[p]), (1, d1[p])] for p in range(2 * ucount)]
    cmine = prescatter(cpieces, "row", cplan)
    cg = lax.all_gather(cmine, "row")

    def cblock(dest, u):
        return jnp.concatenate([cg[dest[2 * u]], cg[dest[2 * u + 1]]], axis=0)

    crow = [[cblock(d, u) for u in range(ucount)] for d in (d0, d1)]

    blk = work[0, :, 0, :]
    shifts = list(range(1, nrow))
    recv = jnp.stack([lax.ppermute(blk, "row", [(0, s), (1, (1 + s) % nrow)]) for s in shifts])
    from0 = lax.dynamic_index_in_dim(recv, jnp.maximum(my_row - 1, 0), keepdims=False)
    from1 = lax.dynamic_index_in_dim(recv, (my_row + nrow - 2) % nrow, keepdims=False)
    a0c = jnp.where(my_row == 0, blk, from0)
    a1c = jnp.where(my_row == 1, blk, from1)
    lead = jnp.concatenate([a0c, a1c], axis=0)
    pcol = work[:, :, 0, :].reshape(tiles * width, width)
    npieces = ncol // 2
    rrows = pcol.shape[0] // npieces
    lrows = lead.shape[0] // npieces
    rplan = [[(0, 2 * q), (1, 2 * q + 1)] for q in range(npieces)]
    rmine = prescatter([pcol[q * rrows:(q + 1) * rrows] for q in range(npieces)], "col", rplan)
    lmine = prescatter([lead[q * lrows:(q + 1) * lrows] for q in range(npieces)], "col", rplan)
    rg = lax.all_gather(jnp.concatenate([rmine, lmine], axis=0), "col")
    rg = rg.reshape(npieces, 2, rrows + lrows, width)

    col0 = rg[:, 0, :rrows].reshape(tiles, width, width)
    col1 = rg[:, 1, :rrows].reshape(tiles, width, width)
    lead0 = rg[:, 0, rrows:].reshape(2 * width, width)
    lead1 = rg[:, 1, rrows:].reshape(2 * width, width)
    a00 = lead0[:width]
    a10 = lead0[width:]
    a11 = lead1[width:]

    block_rows = jnp.arange(tiles, dtype=jnp.int32) * nrow + my_row
    block_cols = jnp.arange(ucount, dtype=jnp.int32) * ncol + my_col
    cT0 = jnp.stack([crow[0][u].T for u in range(ucount)])
    cT1 = jnp.stack([crow[1][u].T for u in range(ucount)])
    eye = jnp.eye(width, dtype=jnp.float32)

    def times_inv_t(y, ginv):
        return jnp.einsum("nab,cb->nac", y, ginv, precision=HIGH,
                          preferred_element_type=jnp.float32)

    g0 = jnp.linalg.cholesky(a00)
    g0i = jax.scipy.linalg.solve_triangular(g0, eye, lower=True)
    x0 = times_inv_t(jnp.concatenate([col0, cT0, a10[None]], axis=0), g0i)
    x0r, x0c, x01 = x0[:tiles], x0[tiles:tiles + ucount], x0[tiles + ucount]
    a11u = a11 - jnp.dot(x01, x01.T, precision=HIGH, preferred_element_type=jnp.float32)
    g1 = jnp.linalg.cholesky(a11u)
    g1i = jax.scipy.linalg.solve_triangular(g1, eye, lower=True)
    y1 = jnp.concatenate([col1, cT1], axis=0) - times_inv_t(
        jnp.concatenate([x0r, x0c], axis=0), x01)
    x1 = times_inv_t(y1, g1i)
    x1r, x1c = x1[:tiles], x1[tiles:]

    left = jnp.concatenate([x0r, x1r], axis=-1).reshape(tiles * width, 2 * width)
    right = jnp.concatenate([x0c, x1c], axis=-1).reshape(ucount * width, 2 * width)
    prod = jnp.dot(left, right.T, precision=HIGH, preferred_element_type=jnp.float32)
    upd = work - prod.reshape(tiles, width, ucount, width)
    irow = block_rows[:, None, None]
    p0r = jnp.where(irow > 0, x0r, jnp.where(irow == 0, g0[None], 0.0))
    p1r = jnp.where(irow > 1, x1r, jnp.where(irow == 1, g1[None], 0.0))
    jcol = block_cols[None, None, :, None]
    upd = jnp.where(block_rows[:, None, None, None] < 2, 0.0, upd)
    work = jnp.where(jcol == 0, p0r[:, :, None, :], jnp.where(jcol == 1, p1r[:, :, None, :], upd))
    return work.reshape(tiles, 1, width, ucount, 1, width)


def solution(mesh):
    in_specs = (P(None, "row", None, None, "col", None),)
    out_specs = P(None, "row", None, None, "col", None)
    return jax.shard_map(
        per_device, mesh=mesh, in_specs=in_specs, out_specs=out_specs, check_vma=False
    )
```

```python
import jax
import jax.numpy as jnp
from jax import lax
from jax.sharding import PartitionSpec as P

HIGH = lax.Precision.HIGHEST


def prescatter(pieces, axis, plan):
    me = lax.axis_index(axis)
    got = jnp.zeros_like(pieces[0])
    for q, pairs in enumerate(plan):
        moved = [(s, d) for s, d in pairs if s != d]
        kept = [s for s, d in pairs if s == d]
        if moved:
            got = got + lax.ppermute(pieces[q], axis, moved)
        for s in kept:
            got = got + jnp.where(me == s, pieces[q], jnp.zeros_like(pieces[q]))
    return got


def per_device(kernel):
    tiles, width, ucount = kernel.shape[0], kernel.shape[2], kernel.shape[3]
    work = kernel.reshape(tiles, width, ucount, width)
    nrow = lax.axis_size("row")
    ncol = lax.axis_size("col")
    my_row = lax.axis_index("row")
    my_col = lax.axis_index("col")
    half = width // 2

    rowblk = work[0]
    cpieces = [rowblk[(p % 2) * half:(p % 2 + 1) * half, p // 2, :] for p in range(2 * ucount)]
    d0 = [(-p) % nrow for p in range(2 * ucount)]
    d1 = [(1 + p) % nrow for p in range(2 * ucount)]
    cplan = [[(0, d0[p]), (1, d1[p])] for p in range(2 * ucount)]
    cmine = prescatter(cpieces, "row", cplan)
    cg = lax.all_gather(cmine, "row")

    def cblock(dest, u):
        return jnp.concatenate([cg[dest[2 * u]], cg[dest[2 * u + 1]]], axis=0)

    crow = [[cblock(d, u) for u in range(ucount)] for d in (d0, d1)]

    blk = work[0, :, 0, :]
    shifts = list(range(1, nrow))
    recv = jnp.stack([lax.ppermute(blk, "row", [(0, s), (1, (1 + s) % nrow)]) for s in shifts])
    from0 = lax.dynamic_index_in_dim(recv, jnp.maximum(my_row - 1, 0), keepdims=False)
    from1 = lax.dynamic_index_in_dim(recv, (my_row + nrow - 2) % nrow, keepdims=False)
    a0c = jnp.where(my_row == 0, blk, from0)
    a1c = jnp.where(my_row == 1, blk, from1)
    eye = jnp.eye(width, dtype=jnp.float32)
    swap = lax.ppermute(jnp.where(my_col == 0, a0c, a1c), "col", [(0, 1), (1, 0)])
    a00 = jnp.where(my_col == 0, a0c, swap)
    a11 = jnp.where(my_col == 0, swap, a1c)
    a10 = jnp.where(my_col == 0, a1c, a0c.T)
    g0 = jnp.linalg.cholesky(a00)
    g0i = jax.scipy.linalg.solve_triangular(g0, eye, lower=True)
    x01 = jnp.dot(a10, g0i.T, precision=HIGH, preferred_element_type=jnp.float32)
    a11u = a11 - jnp.dot(x01, x01.T, precision=HIGH, preferred_element_type=jnp.float32)
    g1 = jnp.linalg.cholesky(a11u)
    g1i = jax.scipy.linalg.solve_triangular(g1, eye, lower=True)
    res = jnp.concatenate([g0i, x01, g1i], axis=0)
    hres = res.shape[0] // 2
    lead = jnp.where(my_col == 0, res[:hres], res[hres:])
    pcol = work[:, :, 0, :].reshape(tiles * width, width)
    npieces = ncol // 2
    rrows = pcol.shape[0] // npieces
    lrows = lead.shape[0] // npieces
    rplan = [[(0, 2 * q), (1, 2 * q + 1)] for q in range(npieces)]
    rmine = prescatter([pcol[q * rrows:(q + 1) * rrows] for q in range(npieces)], "col", rplan)
    lmine = prescatter([lead[q * lrows:(q + 1) * lrows] for q in range(npieces)], "col", rplan)
    rg = lax.all_gather(jnp.concatenate([rmine, lmine], axis=0), "col")
    rg = rg.reshape(npieces, 2, rrows + lrows, width)

    col0 = rg[:, 0, :rrows].reshape(tiles, width, width)
    col1 = rg[:, 1, :rrows].reshape(tiles, width, width)
    resg = jnp.concatenate([rg[:, 0, rrows:].reshape(hres, width),
                            rg[:, 1, rrows:].reshape(hres, width)], axis=0)
    g0i_all = resg[:width]
    x01_all = resg[width:2 * width]
    g1i_all = resg[2 * width:]

    block_rows = jnp.arange(tiles, dtype=jnp.int32) * nrow + my_row
    block_cols = jnp.arange(ucount, dtype=jnp.int32) * ncol + my_col
    cT0 = jnp.stack([crow[0][u].T for u in range(ucount)])
    cT1 = jnp.stack([crow[1][u].T for u in range(ucount)])

    def times_inv_t(y, ginv):
        return jnp.einsum("nab,cb->nac", y, ginv, precision=HIGH,
                          preferred_element_type=jnp.float32)

    x0 = times_inv_t(jnp.concatenate([col0, cT0], axis=0), g0i_all)
    x0r, x0c = x0[:tiles], x0[tiles:]
    y1 = jnp.concatenate([col1, cT1], axis=0) - times_inv_t(x0, x01_all)
    x1 = times_inv_t(y1, g1i_all)
    x1r, x1c = x1[:tiles], x1[tiles:]

    left = jnp.concatenate([x0r, x1r], axis=-1).reshape(tiles * width, 2 * width)
    right = jnp.concatenate([x0c, x1c], axis=-1).reshape(ucount * width, 2 * width)
    prod = jnp.dot(left, right.T, precision=HIGH, preferred_element_type=jnp.float32)
    upd = work - prod.reshape(tiles, width, ucount, width)
    irow = block_rows[:, None, None]
    p0r = jnp.where(irow > 0, x0r, jnp.where(irow == 0, g0[None], 0.0))
    p1r = jnp.where(irow > 1, x1r, jnp.where(irow == 1, g1[None], 0.0))
    jcol = block_cols[None, None, :, None]
    upd = jnp.where(block_rows[:, None, None, None] < 2, 0.0, upd)
    work = jnp.where(jcol == 0, p0r[:, :, None, :], jnp.where(jcol == 1, p1r[:, :, None, :], upd))
    return work.reshape(tiles, 1, width, ucount, 1, width)


def solution(mesh):
    in_specs = (P(None, "row", None, None, "col", None),)
    out_specs = P(None, "row", None, None, "col", None)
    return jax.shard_map(
        per_device, mesh=mesh, in_specs=in_specs, out_specs=out_specs, check_vma=False
    )
```

```python
import jax
import jax.numpy as jnp
from jax import lax
from jax.sharding import PartitionSpec as P

HIGH = lax.Precision.HIGHEST


def prescatter(pieces, axis, plan):
    me = lax.axis_index(axis)
    got = jnp.zeros_like(pieces[0])
    for q, pairs in enumerate(plan):
        moved = [(s, d) for s, d in pairs if s != d]
        kept = [s for s, d in pairs if s == d]
        if moved:
            got = got + lax.ppermute(pieces[q], axis, moved)
        for s in kept:
            got = got + jnp.where(me == s, pieces[q], jnp.zeros_like(pieces[q]))
    return got


def per_device(kernel):
    tiles, width, ucount = kernel.shape[0], kernel.shape[2], kernel.shape[3]
    work = kernel.reshape(tiles, width, ucount, width)
    nrow = lax.axis_size("row")
    ncol = lax.axis_size("col")
    my_row = lax.axis_index("row")
    my_col = lax.axis_index("col")
    half = width // 2

    rowblk = work[0]
    cpieces = [rowblk[(p % 2) * half:(p % 2 + 1) * half, p // 2, :] for p in range(2 * ucount)]
    d0 = [(-p) % nrow for p in range(2 * ucount)]
    d1 = [(1 + p) % nrow for p in range(2 * ucount)]
    cplan = [[(0, d0[p]), (1, d1[p])] for p in range(2 * ucount)]
    cmine = prescatter(cpieces, "row", cplan)
    cg = lax.all_gather(cmine, "row")

    def cblock(dest, u):
        return jnp.concatenate([cg[dest[2 * u]], cg[dest[2 * u + 1]]], axis=0)

    crow = [[cblock(d, u) for u in range(ucount)] for d in (d0, d1)]

    blk = work[0, :, 0, :]
    shifts = list(range(1, nrow))
    recv = jnp.stack([lax.ppermute(blk, "row", [(0, s), (1, (1 + s) % nrow)]) for s in shifts])
    from0 = lax.dynamic_index_in_dim(recv, jnp.maximum(my_row - 1, 0), keepdims=False)
    from1 = lax.dynamic_index_in_dim(recv, (my_row + nrow - 2) % nrow, keepdims=False)
    a0c = jnp.where(my_row == 0, blk, from0)
    a1c = jnp.where(my_row == 1, blk, from1)
    eye = jnp.eye(width, dtype=jnp.float32)
    pcol = work[:, :, 0, :].reshape(tiles * width, width)
    npieces = ncol // 2
    rrows = pcol.shape[0] // npieces
    rplan = [[(0, 2 * q), (1, 2 * q + 1)] for q in range(npieces)]
    rmine = prescatter([pcol[q * rrows:(q + 1) * rrows] for q in range(npieces)], "col", rplan)
    a0c, a1c, rmine = lax.optimization_barrier((a0c, a1c, rmine))
    swap = lax.ppermute(jnp.where(my_col == 0, a0c, a1c), "col", [(0, 1), (1, 0)])
    a00 = jnp.where(my_col == 0, a0c, swap)
    a11 = jnp.where(my_col == 0, swap, a1c)
    a10 = jnp.where(my_col == 0, a1c, a0c.T)
    g0 = jnp.linalg.cholesky(a00)
    g0i = jax.scipy.linalg.solve_triangular(g0, eye, lower=True)
    x01 = jnp.dot(a10, g0i.T, precision=HIGH, preferred_element_type=jnp.float32)
    a11u = a11 - jnp.dot(x01, x01.T, precision=HIGH, preferred_element_type=jnp.float32)
    g1 = jnp.linalg.cholesky(a11u)
    g1i = jax.scipy.linalg.solve_triangular(g1, eye, lower=True)
    res = jnp.concatenate([g0i, x01, g1i], axis=0)
    hres = res.shape[0] // 2
    lead = jnp.where(my_col == 0, res[:hres], res[hres:])
    lrows = lead.shape[0] // npieces
    lmine = prescatter([lead[q * lrows:(q + 1) * lrows] for q in range(npieces)], "col", rplan)
    rg = lax.all_gather(jnp.concatenate([rmine, lmine], axis=0), "col")
    rg = rg.reshape(npieces, 2, rrows + lrows, width)

    col0 = rg[:, 0, :rrows].reshape(tiles, width, width)
    col1 = rg[:, 1, :rrows].reshape(tiles, width, width)
    resg = jnp.concatenate([rg[:, 0, rrows:].reshape(hres, width),
                            rg[:, 1, rrows:].reshape(hres, width)], axis=0)
    g0i_all = resg[:width]
    x01_all = resg[width:2 * width]
    g1i_all = resg[2 * width:]

    block_rows = jnp.arange(tiles, dtype=jnp.int32) * nrow + my_row
    block_cols = jnp.arange(ucount, dtype=jnp.int32) * ncol + my_col
    cT0 = jnp.stack([crow[0][u].T for u in range(ucount)])
    cT1 = jnp.stack([crow[1][u].T for u in range(ucount)])

    def times_inv_t(y, ginv):
        return jnp.einsum("nab,cb->nac", y, ginv, precision=HIGH,
                          preferred_element_type=jnp.float32)

    x0 = times_inv_t(jnp.concatenate([col0, cT0], axis=0), g0i_all)
    x0r, x0c = x0[:tiles], x0[tiles:]
    y1 = jnp.concatenate([col1, cT1], axis=0) - times_inv_t(x0, x01_all)
    x1 = times_inv_t(y1, g1i_all)
    x1r, x1c = x1[:tiles], x1[tiles:]

    rows2d = tiles * width
    prod = jnp.dot(x0r.reshape(rows2d, width), x0c.reshape(ucount * width, width).T,
                   precision=HIGH, preferred_element_type=jnp.float32)
    prod = prod + jnp.dot(x1r.reshape(rows2d, width), x1c.reshape(ucount * width, width).T,
                          precision=HIGH, preferred_element_type=jnp.float32)
    upd = work.reshape(rows2d, ucount * width) - prod
    irow = block_rows[:, None, None]
    p0r = jnp.where(irow > 0, x0r, jnp.where(irow == 0, g0[None], 0.0))
    p1r = jnp.where(irow > 1, x1r, jnp.where(irow == 1, g1[None], 0.0))
    pan = jnp.where(my_col == 0, p0r, p1r).reshape(rows2d, width)
    top = jnp.repeat(block_rows < 2, width)[:, None]
    jcols = jnp.repeat(block_cols, width)[None, :]
    upd = jnp.where(top & (jcols >= 2), 0.0, upd)
    first = jnp.where(my_col < 2, pan, upd[:, :width])
    out = jnp.concatenate([first, upd[:, width:]], axis=1)
    return out.reshape(tiles, 1, width, ucount, 1, width)


def solution(mesh):
    in_specs = (P(None, "row", None, None, "col", None),)
    out_specs = P(None, "row", None, None, "col", None)
    return jax.shard_map(
        per_device, mesh=mesh, in_specs=in_specs, out_specs=out_specs, check_vma=False
    )
```

```python
import jax
import jax.numpy as jnp
from jax import lax
from jax.sharding import PartitionSpec as P

HIGH = lax.Precision.HIGHEST


def per_device(kernel):
    tiles, width, ucount = kernel.shape[0], kernel.shape[2], kernel.shape[3]
    work = kernel.reshape(tiles, width, ucount, width)
    nrow = lax.axis_size("row")
    ncol = lax.axis_size("col")
    my_row = lax.axis_index("row")
    my_col = lax.axis_index("col")
    half = width // 2

    rowblk = work[0]
    shifts = list(range(1, nrow))
    recv = jnp.stack([lax.ppermute(rowblk, "row", [(0, s), (1, (1 + s) % nrow)]) for s in shifts])
    from0 = lax.dynamic_index_in_dim(recv, jnp.maximum(my_row - 1, 0), keepdims=False)
    from1 = lax.dynamic_index_in_dim(recv, (my_row + nrow - 2) % nrow, keepdims=False)
    r0 = jnp.where(my_row == 0, rowblk, from0)
    r1 = jnp.where(my_row == 1, rowblk, from1)
    crow = [[r[:, u, :] for u in range(ucount)] for r in (r0, r1)]
    a0c = crow[0][0]
    a1c = crow[1][0]
    eye = jnp.eye(width, dtype=jnp.float32)
    pcol = work[:, :, 0, :].reshape(tiles * width, width)
    npieces = ncol // 2
    rrows = pcol.shape[0] // npieces
    rel = pcol.reshape(npieces, rrows, width)
    q = my_col // 2
    span = npieces // 2
    while span >= 1:
        pairs = [(2 * h + k, 2 * (h + span) + k) for h in range(0, npieces, 2 * span) for k in range(2)]
        got = lax.ppermute(rel[span:2 * span], "col", pairs)
        rel = jnp.where(q % (2 * span) == span, got, rel[:span])
        span //= 2
    rmine = rel[0]
    swap = lax.ppermute(jnp.where(my_col == 0, a0c, a1c), "col", [(0, 1), (1, 0)])
    a00 = jnp.where(my_col == 0, a0c, swap)
    a11 = jnp.where(my_col == 0, swap, a1c)
    a10 = jnp.where(my_col == 0, a1c, a0c.T)
    g0 = jnp.linalg.cholesky(a00)
    g0i = jax.scipy.linalg.solve_triangular(g0, eye, lower=True)
    x01 = jnp.dot(a10, g0i.T, precision=HIGH, preferred_element_type=jnp.float32)
    a11u = a11 - jnp.dot(x01, x01.T, precision=HIGH, preferred_element_type=jnp.float32)
    g1 = jnp.linalg.cholesky(a11u)
    g1i = jax.scipy.linalg.solve_triangular(g1, eye, lower=True)
    res = jnp.concatenate([g0i, x01, g1i], axis=0)
    shift = 2
    while shift < ncol:
        got = lax.ppermute(res, "col", [(d, d + shift) for d in range(shift)])
        res = jnp.where((my_col >= shift) & (my_col < 2 * shift), got, res)
        shift *= 2
    rg = lax.all_gather(rmine, "col")
    rg = rg.reshape(npieces, 2, rrows, width)

    col0 = rg[:, 0].reshape(tiles, width, width)
    col1 = rg[:, 1].reshape(tiles, width, width)
    g0i_all = res[:width]
    x01_all = res[width:2 * width]
    g1i_all = res[2 * width:]

    block_rows = jnp.arange(tiles, dtype=jnp.int32) * nrow + my_row
    block_cols = jnp.arange(ucount, dtype=jnp.int32) * ncol + my_col
    cT0 = jnp.stack([crow[0][u].T for u in range(ucount)])
    cT1 = jnp.stack([crow[1][u].T for u in range(ucount)])

    def times_inv_t(y, ginv):
        return jnp.einsum("nab,cb->nac", y, ginv, precision=HIGH,
                          preferred_element_type=jnp.float32)

    x0 = times_inv_t(jnp.concatenate([col0, cT0], axis=0), g0i_all)
    x0r, x0c = x0[:tiles], x0[tiles:]
    y1 = jnp.concatenate([col1, cT1], axis=0) - times_inv_t(x0, x01_all)
    x1 = times_inv_t(y1, g1i_all)
    x1r, x1c = x1[:tiles], x1[tiles:]

    rows2d = tiles * width
    prod = jnp.dot(x0r.reshape(rows2d, width), x0c.reshape(ucount * width, width).T,
                   precision=HIGH, preferred_element_type=jnp.float32)
    prod = prod + jnp.dot(x1r.reshape(rows2d, width), x1c.reshape(ucount * width, width).T,
                          precision=HIGH, preferred_element_type=jnp.float32)
    upd = work.reshape(rows2d, ucount * width) - prod
    irow = block_rows[:, None, None]
    p0r = jnp.where(irow > 0, x0r, jnp.where(irow == 0, g0[None], 0.0))
    p1r = jnp.where(irow > 1, x1r, jnp.where(irow == 1, g1[None], 0.0))
    pan = jnp.where(my_col == 0, p0r, p1r).reshape(rows2d, width)
    top = jnp.repeat(block_rows < 2, width)[:, None]
    jcols = jnp.repeat(block_cols, width)[None, :]
    upd = jnp.where(top & (jcols >= 2), 0.0, upd)
    first = jnp.where(my_col < 2, pan, upd[:, :width])
    out = jnp.concatenate([first, upd[:, width:]], axis=1)
    return out.reshape(tiles, 1, width, ucount, 1, width)


def solution(mesh):
    in_specs = (P(None, "row", None, None, "col", None),)
    out_specs = P(None, "row", None, None, "col", None)
    return jax.shard_map(
        per_device, mesh=mesh, in_specs=in_specs, out_specs=out_specs, check_vma=False
    )
```

```python
import jax
import jax.numpy as jnp
from jax import lax
from jax.sharding import PartitionSpec as P

HIGH = lax.Precision.HIGHEST


def prescatter(pieces, axis, plan):
    me = lax.axis_index(axis)
    got = jnp.zeros_like(pieces[0])
    for q, pairs in enumerate(plan):
        moved = [(s, d) for s, d in pairs if s != d]
        kept = [s for s, d in pairs if s == d]
        if moved:
            got = got + lax.ppermute(pieces[q], axis, moved)
        for s in kept:
            got = got + jnp.where(me == s, pieces[q], jnp.zeros_like(pieces[q]))
    return got


def per_device(kernel):
    tiles, width, ucount = kernel.shape[0], kernel.shape[2], kernel.shape[3]
    w2d = kernel.reshape(tiles * width, ucount * width)
    w3d = w2d.reshape(tiles, width, ucount * width)
    nrow = lax.axis_size("row")
    ncol = lax.axis_size("col")
    my_row = lax.axis_index("row")
    my_col = lax.axis_index("col")
    half = width // 2

    rowblk = w2d[:width]
    cpieces = [rowblk[(p % 2) * half:(p % 2 + 1) * half, (p // 2) * width:(p // 2 + 1) * width]
               for p in range(2 * ucount)]
    d0 = [(-p) % nrow for p in range(2 * ucount)]
    d1 = [(1 + p) % nrow for p in range(2 * ucount)]
    cplan = [[(0, d0[p]), (1, d1[p])] for p in range(2 * ucount)]
    cmine = prescatter(cpieces, "row", cplan)
    cg = lax.all_gather(cmine, "row")

    def cblock(dest, u):
        return jnp.concatenate([cg[dest[2 * u]], cg[dest[2 * u + 1]]], axis=0)

    crow = [[cblock(d, u) for u in range(ucount)] for d in (d0, d1)]

    blk = rowblk[:, :width]
    shifts = list(range(1, nrow))
    recv = jnp.stack([lax.ppermute(blk, "row", [(0, s), (1, (1 + s) % nrow)]) for s in shifts])
    from0 = lax.dynamic_index_in_dim(recv, jnp.maximum(my_row - 1, 0), keepdims=False)
    from1 = lax.dynamic_index_in_dim(recv, (my_row + nrow - 2) % nrow, keepdims=False)
    a0c = jnp.where(my_row == 0, blk, from0)
    a1c = jnp.where(my_row == 1, blk, from1)
    eye = jnp.eye(width, dtype=jnp.float32)
    pcol = w3d[:, :, :width].reshape(tiles * width, width)
    npieces = ncol // 2
    rrows = pcol.shape[0] // npieces
    rel = pcol.reshape(npieces, rrows, width)
    q = my_col // 2
    span = npieces // 2
    while span >= 1:
        pairs = [(2 * h + k, 2 * (h + span) + k) for h in range(0, npieces, 2 * span) for k in range(2)]
        got = lax.ppermute(rel[span:2 * span], "col", pairs)
        rel = jnp.where(q % (2 * span) == span, got, rel[:span])
        span //= 2
    rmine = rel[0]
    swap = lax.ppermute(jnp.where(my_col == 0, a0c, a1c), "col", [(0, 1), (1, 0)])
    a00 = jnp.where(my_col == 0, a0c, swap)
    a11 = jnp.where(my_col == 0, swap, a1c)
    a10 = jnp.where(my_col == 0, a1c, a0c.T)
    g0 = jnp.linalg.cholesky(a00)
    g0i = jax.scipy.linalg.solve_triangular(g0, eye, lower=True)
    x01 = jnp.dot(a10, g0i.T, precision=HIGH, preferred_element_type=jnp.float32)
    a11u = a11 - jnp.dot(x01, x01.T, precision=HIGH, preferred_element_type=jnp.float32)
    g1 = jnp.linalg.cholesky(a11u)
    g1i = jax.scipy.linalg.solve_triangular(g1, eye, lower=True)
    res = jnp.concatenate([g0i, x01, g1i], axis=0)
    hres = res.shape[0] // 2
    lead = jnp.where(my_col == 0, res[:hres], res[hres:])
    lrows = lead.shape[0] // npieces
    rplan = [[(0, 2 * h), (1, 2 * h + 1)] for h in range(npieces)]
    lmine = prescatter([lead[h * lrows:(h + 1) * lrows] for h in range(npieces)], "col", rplan)
    rg = lax.all_gather(jnp.concatenate([rmine, lmine], axis=0), "col")
    rg = rg.reshape(npieces, 2, rrows + lrows, width)

    col0 = rg[:, 0, :rrows].reshape(tiles, width, width)
    col1 = rg[:, 1, :rrows].reshape(tiles, width, width)
    resg = jnp.concatenate([rg[:, 0, rrows:].reshape(hres, width),
                            rg[:, 1, rrows:].reshape(hres, width)], axis=0)
    g0i_all = resg[:width]
    x01_all = resg[width:2 * width]
    g1i_all = resg[2 * width:]

    block_rows = jnp.arange(tiles, dtype=jnp.int32) * nrow + my_row
    block_cols = jnp.arange(ucount, dtype=jnp.int32) * ncol + my_col
    cT0 = jnp.stack([crow[0][u].T for u in range(ucount)])
    cT1 = jnp.stack([crow[1][u].T for u in range(ucount)])

    def times_inv_t(y, ginv):
        return jnp.einsum("nab,cb->nac", y, ginv, precision=HIGH,
                          preferred_element_type=jnp.float32)

    x0 = times_inv_t(jnp.concatenate([col0, cT0], axis=0), g0i_all)
    x0r, x0c = x0[:tiles], x0[tiles:]
    y1 = jnp.concatenate([col1, cT1], axis=0) - times_inv_t(x0, x01_all)
    x1 = times_inv_t(y1, g1i_all)
    x1r, x1c = x1[:tiles], x1[tiles:]

    rows2d = tiles * width
    prod = jnp.dot(x0r.reshape(rows2d, width), x0c.reshape(ucount * width, width).T,
                   precision=HIGH, preferred_element_type=jnp.float32)
    prod = prod + jnp.dot(x1r.reshape(rows2d, width), x1c.reshape(ucount * width, width).T,
                          precision=HIGH, preferred_element_type=jnp.float32)
    upd = w2d - prod
    irow = block_rows[:, None, None]
    p0r = jnp.where(irow > 0, x0r, jnp.where(irow == 0, g0[None], 0.0))
    p1r = jnp.where(irow > 1, x1r, jnp.where(irow == 1, g1[None], 0.0))
    pan = jnp.where(my_col == 0, p0r, p1r).reshape(rows2d, width)
    top = jnp.repeat(block_rows < 2, width)[:, None]
    jcols = jnp.repeat(block_cols, width)[None, :]
    upd = jnp.where(top & (jcols >= 2), 0.0, upd)
    first = jnp.where(my_col < 2, pan, upd[:, :width])
    out = jnp.concatenate([first, upd[:, width:]], axis=1)
    return out.reshape(tiles, 1, width, ucount, 1, width)


def solution(mesh):
    in_specs = (P(None, "row", None, None, "col", None),)
    out_specs = P(None, "row", None, None, "col", None)
    return jax.shard_map(
        per_device, mesh=mesh, in_specs=in_specs, out_specs=out_specs, check_vma=False
    )
```

```python
import jax
import jax.numpy as jnp
from jax import lax
from jax.sharding import PartitionSpec as P

HIGH = lax.Precision.HIGHEST


def prescatter(pieces, axis, plan):
    me = lax.axis_index(axis)
    got = jnp.zeros_like(pieces[0])
    for q, pairs in enumerate(plan):
        moved = [(s, d) for s, d in pairs if s != d]
        kept = [s for s, d in pairs if s == d]
        if moved:
            got = got + lax.ppermute(pieces[q], axis, moved)
        for s in kept:
            got = got + jnp.where(me == s, pieces[q], jnp.zeros_like(pieces[q]))
    return got


def per_device(kernel):
    tiles, width, ucount = kernel.shape[0], kernel.shape[2], kernel.shape[3]
    w2d = kernel.reshape(tiles * width, ucount * width)
    w3d = w2d.reshape(tiles, width, ucount * width)
    nrow = lax.axis_size("row")
    ncol = lax.axis_size("col")
    my_row = lax.axis_index("row")
    my_col = lax.axis_index("col")
    half = width // 2

    rowblk = w2d[:width]
    cpieces = [rowblk[(p % 2) * half:(p % 2 + 1) * half, (p // 2) * width:(p // 2 + 1) * width]
               for p in range(2 * ucount)]
    d0 = [(-p) % nrow for p in range(2 * ucount)]
    d1 = [(1 + p) % nrow for p in range(2 * ucount)]
    cplan = [[(0, d0[p]), (1, d1[p])] for p in range(2 * ucount)]
    cmine = prescatter(cpieces, "row", cplan)
    cg = lax.all_gather(cmine, "row")

    def cblock(dest, u):
        return jnp.concatenate([cg[dest[2 * u]], cg[dest[2 * u + 1]]], axis=0)

    crow = [[cblock(d, u) for u in range(ucount)] for d in (d0, d1)]

    blk = rowblk[:, :width]
    shifts = list(range(1, nrow))
    recv = jnp.stack([lax.ppermute(blk, "row", [(0, s), (1, (1 + s) % nrow)]) for s in shifts])
    from0 = lax.dynamic_index_in_dim(recv, jnp.maximum(my_row - 1, 0), keepdims=False)
    from1 = lax.dynamic_index_in_dim(recv, (my_row + nrow - 2) % nrow, keepdims=False)
    a0c = jnp.where(my_row == 0, blk, from0)
    a1c = jnp.where(my_row == 1, blk, from1)
    eye = jnp.eye(width, dtype=jnp.float32)
    pcol = w3d[:, :, :width].reshape(tiles * width, width)
    npieces = ncol // 2
    rrows = pcol.shape[0] // npieces
    rel = pcol.reshape(npieces, rrows, width)
    q = my_col // 2

    def tree_round(rel, span):
        pairs = [(2 * h + k, 2 * (h + span) + k) for h in range(0, npieces, 2 * span) for k in range(2)]
        got = lax.ppermute(rel[span:2 * span], "col", pairs)
        return jnp.where(q % (2 * span) == span, got, rel[:span])

    spans = [npieces // 2 ** (i + 1) for i in range(4)]
    rel = tree_round(rel, spans[0])
    swap = lax.ppermute(jnp.where(my_col == 0, a0c, a1c), "col", [(0, 1), (1, 0)])
    a00 = jnp.where(my_col == 0, a0c, swap)
    a11 = jnp.where(my_col == 0, swap, a1c)
    a10 = jnp.where(my_col == 0, a1c, a0c.T)
    rel, a00 = lax.optimization_barrier((rel, a00))
    g0 = jnp.linalg.cholesky(a00)
    rel = tree_round(rel, spans[1])
    rel, g0 = lax.optimization_barrier((rel, g0))
    g0i = jax.scipy.linalg.solve_triangular(g0, eye, lower=True)
    rel = tree_round(rel, spans[2])
    rel, g0i = lax.optimization_barrier((rel, g0i))
    x01 = jnp.dot(a10, g0i.T, precision=HIGH, preferred_element_type=jnp.float32)
    a11u = a11 - jnp.dot(x01, x01.T, precision=HIGH, preferred_element_type=jnp.float32)
    g1 = jnp.linalg.cholesky(a11u)
    rel = tree_round(rel, spans[3])
    rel, g1 = lax.optimization_barrier((rel, g1))
    g1i = jax.scipy.linalg.solve_triangular(g1, eye, lower=True)
    rmine = rel[0]
    res = jnp.concatenate([g0i, x01, g1i], axis=0)
    hres = res.shape[0] // 2
    lead = jnp.where(my_col == 0, res[:hres], res[hres:])
    lrows = lead.shape[0] // npieces
    rplan = [[(0, 2 * h), (1, 2 * h + 1)] for h in range(npieces)]
    lmine = prescatter([lead[h * lrows:(h + 1) * lrows] for h in range(npieces)], "col", rplan)
    rg = lax.all_gather(jnp.concatenate([rmine, lmine], axis=0), "col")
    rg = rg.reshape(npieces, 2, rrows + lrows, width)

    col0 = rg[:, 0, :rrows].reshape(tiles, width, width)
    col1 = rg[:, 1, :rrows].reshape(tiles, width, width)
    resg = jnp.concatenate([rg[:, 0, rrows:].reshape(hres, width),
                            rg[:, 1, rrows:].reshape(hres, width)], axis=0)
    g0i_all = resg[:width]
    x01_all = resg[width:2 * width]
    g1i_all = resg[2 * width:]

    block_rows = jnp.arange(tiles, dtype=jnp.int32) * nrow + my_row
    block_cols = jnp.arange(ucount, dtype=jnp.int32) * ncol + my_col
    cT0 = jnp.stack([crow[0][u].T for u in range(ucount)])
    cT1 = jnp.stack([crow[1][u].T for u in range(ucount)])

    def times_inv_t(y, ginv):
        return jnp.einsum("nab,cb->nac", y, ginv, precision=HIGH,
                          preferred_element_type=jnp.float32)

    x0 = times_inv_t(jnp.concatenate([col0, cT0], axis=0), g0i_all)
    x0r, x0c = x0[:tiles], x0[tiles:]
    y1 = jnp.concatenate([col1, cT1], axis=0) - times_inv_t(x0, x01_all)
    x1 = times_inv_t(y1, g1i_all)
    x1r, x1c = x1[:tiles], x1[tiles:]

    rows2d = tiles * width
    prod = jnp.dot(x0r.reshape(rows2d, width), x0c.reshape(ucount * width, width).T,
                   precision=HIGH, preferred_element_type=jnp.float32)
    prod = prod + jnp.dot(x1r.reshape(rows2d, width), x1c.reshape(ucount * width, width).T,
                          precision=HIGH, preferred_element_type=jnp.float32)
    upd = w2d - prod
    irow = block_rows[:, None, None]
    p0r = jnp.where(irow > 0, x0r, jnp.where(irow == 0, g0[None], 0.0))
    p1r = jnp.where(irow > 1, x1r, jnp.where(irow == 1, g1[None], 0.0))
    pan = jnp.where(my_col == 0, p0r, p1r).reshape(rows2d, width)
    top = jnp.repeat(block_rows < 2, width)[:, None]
    jcols = jnp.repeat(block_cols, width)[None, :]
    upd = jnp.where(top & (jcols >= 2), 0.0, upd)
    first = jnp.where(my_col < 2, pan, upd[:, :width])
    out = jnp.concatenate([first, upd[:, width:]], axis=1)
    return out.reshape(tiles, 1, width, ucount, 1, width)


def solution(mesh):
    in_specs = (P(None, "row", None, None, "col", None),)
    out_specs = P(None, "row", None, None, "col", None)
    return jax.shard_map(
        per_device, mesh=mesh, in_specs=in_specs, out_specs=out_specs, check_vma=False
    )
```

```python
import jax
import jax.numpy as jnp
from jax import lax
from jax.sharding import PartitionSpec as P

HIGH = lax.Precision.HIGHEST


def prescatter(pieces, axis, plan):
    me = lax.axis_index(axis)
    got = jnp.zeros_like(pieces[0])
    for q, pairs in enumerate(plan):
        moved = [(s, d) for s, d in pairs if s != d]
        kept = [s for s, d in pairs if s == d]
        if moved:
            got = got + lax.ppermute(pieces[q], axis, moved)
        for s in kept:
            got = got + jnp.where(me == s, pieces[q], jnp.zeros_like(pieces[q]))
    return got


def mm(a, b):
    return jnp.dot(a, b, precision=HIGH, preferred_element_type=jnp.float32)


def chol_and_inverse(a):
    a = (a + a.T) * 0.5
    h = a.shape[0] // 2
    eye = jnp.eye(h, dtype=a.dtype)
    l11 = jnp.tril(lax.linalg.cholesky(a[:h, :h], symmetrize_input=False))
    i11 = jax.scipy.linalg.solve_triangular(l11, eye, lower=True)
    l21 = mm(a[h:, :h], i11.T)
    s = a[h:, h:] - mm(l21, l21.T)
    s = (s + s.T) * 0.5
    l22 = jnp.tril(lax.linalg.cholesky(s, symmetrize_input=False))
    i22 = jax.scipy.linalg.solve_triangular(l22, eye, lower=True)
    i21 = -mm(i22, mm(l21, i11))
    zero = jnp.zeros((h, h), a.dtype)
    g = jnp.concatenate([jnp.concatenate([l11, zero], axis=1),
                         jnp.concatenate([l21, l22], axis=1)], axis=0)
    gi = jnp.concatenate([jnp.concatenate([i11, zero], axis=1),
                          jnp.concatenate([i21, i22], axis=1)], axis=0)
    return g, gi


def per_device(kernel):
    tiles, width, ucount = kernel.shape[0], kernel.shape[2], kernel.shape[3]
    work = kernel.reshape(tiles, width, ucount, width)
    nrow = lax.axis_size("row")
    ncol = lax.axis_size("col")
    my_row = lax.axis_index("row")
    my_col = lax.axis_index("col")
    half = width // 2

    rowblk = work[0]
    cpieces = [rowblk[(p % 2) * half:(p % 2 + 1) * half, p // 2, :] for p in range(2 * ucount)]
    d0 = [(-p) % nrow for p in range(2 * ucount)]
    d1 = [(1 + p) % nrow for p in range(2 * ucount)]
    cplan = [[(0, d0[p]), (1, d1[p])] for p in range(2 * ucount)]
    cmine = prescatter(cpieces, "row", cplan)
    cg = lax.all_gather(cmine, "row")

    def cblock(dest, u):
        return jnp.concatenate([cg[dest[2 * u]], cg[dest[2 * u + 1]]], axis=0)

    crow = [[cblock(d, u) for u in range(ucount)] for d in (d0, d1)]

    blk = work[0, :, 0, :]
    shifts = list(range(1, nrow))
    recv = jnp.stack([lax.ppermute(blk, "row", [(0, s), (1, (1 + s) % nrow)]) for s in shifts])
    from0 = lax.dynamic_index_in_dim(recv, jnp.maximum(my_row - 1, 0), keepdims=False)
    from1 = lax.dynamic_index_in_dim(recv, (my_row + nrow - 2) % nrow, keepdims=False)
    a0c = jnp.where(my_row == 0, blk, from0)
    a1c = jnp.where(my_row == 1, blk, from1)
    eye = jnp.eye(width, dtype=jnp.float32)
    pcol = work[:, :, 0, :].reshape(tiles * width, width)
    npieces = ncol // 2
    rrows = pcol.shape[0] // npieces
    rplan = [[(0, 2 * q), (1, 2 * q + 1)] for q in range(npieces)]
    rmine = prescatter([pcol[q * rrows:(q + 1) * rrows] for q in range(npieces)], "col", rplan)
    a0c, a1c, rmine = lax.optimization_barrier((a0c, a1c, rmine))
    swap = lax.ppermute(jnp.where(my_col == 0, a0c, a1c), "col", [(0, 1), (1, 0)])
    a00 = jnp.where(my_col == 0, a0c, swap)
    a11 = jnp.where(my_col == 0, swap, a1c)
    a10 = jnp.where(my_col == 0, a1c, a0c.T)
    g0, g0i = chol_and_inverse(a00)
    x01 = jnp.dot(a10, g0i.T, precision=HIGH, preferred_element_type=jnp.float32)
    a11u = a11 - jnp.dot(x01, x01.T, precision=HIGH, preferred_element_type=jnp.float32)
    g1, g1i = chol_and_inverse(a11u)
    res = jnp.concatenate([g0i, x01, g1i], axis=0)
    hres = res.shape[0] // 2
    lead = jnp.where(my_col == 0, res[:hres], res[hres:])
    lrows = lead.shape[0] // npieces
    lmine = prescatter([lead[q * lrows:(q + 1) * lrows] for q in range(npieces)], "col", rplan)
    rg = lax.all_gather(jnp.concatenate([rmine, lmine], axis=0), "col")
    rg = rg.reshape(npieces, 2, rrows + lrows, width)

    col0 = rg[:, 0, :rrows].reshape(tiles, width, width)
    col1 = rg[:, 1, :rrows].reshape(tiles, width, width)
    resg = jnp.concatenate([rg[:, 0, rrows:].reshape(hres, width),
                            rg[:, 1, rrows:].reshape(hres, width)], axis=0)
    g0i_all = resg[:width]
    x01_all = resg[width:2 * width]
    g1i_all = resg[2 * width:]

    block_rows = jnp.arange(tiles, dtype=jnp.int32) * nrow + my_row
    block_cols = jnp.arange(ucount, dtype=jnp.int32) * ncol + my_col
    cT0 = jnp.stack([crow[0][u].T for u in range(ucount)])
    cT1 = jnp.stack([crow[1][u].T for u in range(ucount)])

    def times_inv_t(y, ginv):
        return jnp.einsum("nab,cb->nac", y, ginv, precision=HIGH,
                          preferred_element_type=jnp.float32)

    x0 = times_inv_t(jnp.concatenate([col0, cT0], axis=0), g0i_all)
    x0r, x0c = x0[:tiles], x0[tiles:]
    y1 = jnp.concatenate([col1, cT1], axis=0) - times_inv_t(x0, x01_all)
    x1 = times_inv_t(y1, g1i_all)
    x1r, x1c = x1[:tiles], x1[tiles:]

    rows2d = tiles * width
    prod = jnp.dot(x0r.reshape(rows2d, width), x0c.reshape(ucount * width, width).T,
                   precision=HIGH, preferred_element_type=jnp.float32)
    prod = prod + jnp.dot(x1r.reshape(rows2d, width), x1c.reshape(ucount * width, width).T,
                          precision=HIGH, preferred_element_type=jnp.float32)
    upd = work.reshape(rows2d, ucount * width) - prod
    irow = block_rows[:, None, None]
    p0r = jnp.where(irow > 0, x0r, jnp.where(irow == 0, g0[None], 0.0))
    p1r = jnp.where(irow > 1, x1r, jnp.where(irow == 1, g1[None], 0.0))
    pan = jnp.where(my_col == 0, p0r, p1r).reshape(rows2d, width)
    top = jnp.repeat(block_rows < 2, width)[:, None]
    jcols = jnp.repeat(block_cols, width)[None, :]
    upd = jnp.where(top & (jcols >= 2), 0.0, upd)
    first = jnp.where(my_col < 2, pan, upd[:, :width])
    out = jnp.concatenate([first, upd[:, width:]], axis=1)
    return out.reshape(tiles, 1, width, ucount, 1, width)


def solution(mesh):
    in_specs = (P(None, "row", None, None, "col", None),)
    out_specs = P(None, "row", None, None, "col", None)
    return jax.shard_map(
        per_device, mesh=mesh, in_specs=in_specs, out_specs=out_specs, check_vma=False
    )
```

```python
import jax
import jax.numpy as jnp
from jax import lax
from jax.sharding import PartitionSpec as P

HIGH = lax.Precision.HIGHEST


def prescatter(pieces, axis, plan):
    me = lax.axis_index(axis)
    got = jnp.zeros_like(pieces[0])
    for q, pairs in enumerate(plan):
        moved = [(s, d) for s, d in pairs if s != d]
        kept = [s for s, d in pairs if s == d]
        if moved:
            got = got + lax.ppermute(pieces[q], axis, moved)
        for s in kept:
            got = got + jnp.where(me == s, pieces[q], jnp.zeros_like(pieces[q]))
    return got


def mm(a, b):
    return jnp.dot(a, b, precision=HIGH, preferred_element_type=jnp.float32)


def chol_and_inverse(a):
    a = (a + a.T) * 0.5
    h = a.shape[0] // 2
    eye = jnp.eye(h, dtype=a.dtype)
    l11 = jnp.tril(lax.linalg.cholesky(a[:h, :h], symmetrize_input=False))
    i11 = jax.scipy.linalg.solve_triangular(l11, eye, lower=True)
    l21 = mm(a[h:, :h], i11.T)
    s = a[h:, h:] - mm(l21, l21.T)
    s = (s + s.T) * 0.5
    l22 = jnp.tril(lax.linalg.cholesky(s, symmetrize_input=False))
    i22 = jax.scipy.linalg.solve_triangular(l22, eye, lower=True)
    i21 = -mm(i22, mm(l21, i11))
    zero = jnp.zeros((h, h), a.dtype)
    g = jnp.concatenate([jnp.concatenate([l11, zero], axis=1),
                         jnp.concatenate([l21, l22], axis=1)], axis=0)
    gi = jnp.concatenate([jnp.concatenate([i11, zero], axis=1),
                          jnp.concatenate([i21, i22], axis=1)], axis=0)
    return g, gi


def per_device(kernel):
    tiles, width, ucount = kernel.shape[0], kernel.shape[2], kernel.shape[3]
    work = kernel.reshape(tiles, width, ucount, width)
    nrow = lax.axis_size("row")
    ncol = lax.axis_size("col")
    my_row = lax.axis_index("row")
    my_col = lax.axis_index("col")
    half = width // 2

    rowblk = kernel[0, 0, :, :, 0, :]
    cpieces = [rowblk[(p % 2) * half:(p % 2 + 1) * half, p // 2, :] for p in range(2 * ucount)]
    d0 = [(-p) % nrow for p in range(2 * ucount)]
    d1 = [(1 + p) % nrow for p in range(2 * ucount)]
    cplan = [[(0, d0[p]), (1, d1[p])] for p in range(2 * ucount)]
    cmine = prescatter(cpieces, "row", cplan)
    cg = lax.all_gather(cmine, "row")

    def cblock(dest, u):
        return jnp.concatenate([cg[dest[2 * u]], cg[dest[2 * u + 1]]], axis=0)

    crow = [[cblock(d, u) for u in range(ucount)] for d in (d0, d1)]

    blk = kernel[0, 0, :, 0, 0, :]
    shifts = list(range(1, nrow))
    recv = jnp.stack([lax.ppermute(blk, "row", [(0, s), (1, (1 + s) % nrow)]) for s in shifts])
    from0 = lax.dynamic_index_in_dim(recv, jnp.maximum(my_row - 1, 0), keepdims=False)
    from1 = lax.dynamic_index_in_dim(recv, (my_row + nrow - 2) % nrow, keepdims=False)
    a0c = jnp.where(my_row == 0, blk, from0)
    a1c = jnp.where(my_row == 1, blk, from1)
    eye = jnp.eye(width, dtype=jnp.float32)
    pcol = kernel[:, 0, :, 0, 0, :].reshape(tiles * width, width)
    npieces = ncol // 2
    rrows = pcol.shape[0] // npieces
    rplan = [[(0, 2 * q), (1, 2 * q + 1)] for q in range(npieces)]
    rmine = prescatter([pcol[q * rrows:(q + 1) * rrows] for q in range(npieces)], "col", rplan)
    a0c, a1c, rmine = lax.optimization_barrier((a0c, a1c, rmine))
    swap = lax.ppermute(jnp.where(my_col == 0, a0c, a1c), "col", [(0, 1), (1, 0)])
    a00 = jnp.where(my_col == 0, a0c, swap)
    a11 = jnp.where(my_col == 0, swap, a1c)
    a10 = jnp.where(my_col == 0, a1c, a0c.T)
    g0, g0i = chol_and_inverse(a00)
    x01 = jnp.dot(a10, g0i.T, precision=HIGH, preferred_element_type=jnp.float32)
    a11u = a11 - jnp.dot(x01, x01.T, precision=HIGH, preferred_element_type=jnp.float32)
    g1, g1i = chol_and_inverse(a11u)
    res = jnp.concatenate([g0i, x01, g1i], axis=0)
    hres = res.shape[0] // 2
    lead = jnp.where(my_col == 0, res[:hres], res[hres:])
    lrows = lead.shape[0] // npieces
    lmine = prescatter([lead[q * lrows:(q + 1) * lrows] for q in range(npieces)], "col", rplan)
    rg = lax.all_gather(jnp.concatenate([rmine, lmine], axis=0), "col")
    rg = rg.reshape(npieces, 2, rrows + lrows, width)

    col0 = rg[:, 0, :rrows].reshape(tiles, width, width)
    col1 = rg[:, 1, :rrows].reshape(tiles, width, width)
    resg = jnp.concatenate([rg[:, 0, rrows:].reshape(hres, width),
                            rg[:, 1, rrows:].reshape(hres, width)], axis=0)
    g0i_all = resg[:width]
    x01_all = resg[width:2 * width]
    g1i_all = resg[2 * width:]

    block_rows = jnp.arange(tiles, dtype=jnp.int32) * nrow + my_row
    block_cols = jnp.arange(ucount, dtype=jnp.int32) * ncol + my_col
    cT0 = jnp.stack([crow[0][u].T for u in range(ucount)])
    cT1 = jnp.stack([crow[1][u].T for u in range(ucount)])

    def times_inv_t(y, ginv):
        return jnp.einsum("nab,cb->nac", y, ginv, precision=HIGH,
                          preferred_element_type=jnp.float32)

    x0 = times_inv_t(jnp.concatenate([col0, cT0], axis=0), g0i_all)
    x0r, x0c = x0[:tiles], x0[tiles:]
    y1 = jnp.concatenate([col1, cT1], axis=0) - times_inv_t(x0, x01_all)
    x1 = times_inv_t(y1, g1i_all)
    x1r, x1c = x1[:tiles], x1[tiles:]

    rows2d = tiles * width
    prod = jnp.dot(x0r.reshape(rows2d, width), x0c.reshape(ucount * width, width).T,
                   precision=HIGH, preferred_element_type=jnp.float32)
    prod = prod + jnp.dot(x1r.reshape(rows2d, width), x1c.reshape(ucount * width, width).T,
                          precision=HIGH, preferred_element_type=jnp.float32)
    upd = work.reshape(rows2d, ucount * width) - prod
    irow = block_rows[:, None, None]
    p0r = jnp.where(irow > 0, x0r, jnp.where(irow == 0, g0[None], 0.0))
    p1r = jnp.where(irow > 1, x1r, jnp.where(irow == 1, g1[None], 0.0))
    pan = jnp.where(my_col == 0, p0r, p1r).reshape(rows2d, width)
    top = jnp.repeat(block_rows < 2, width)[:, None]
    jcols = jnp.repeat(block_cols, width)[None, :]
    upd = jnp.where(top & (jcols >= 2), 0.0, upd)
    first = jnp.where(my_col < 2, pan, upd[:, :width])
    out = jnp.concatenate([first, upd[:, width:]], axis=1)
    return out.reshape(tiles, 1, width, ucount, 1, width)


def solution(mesh):
    in_specs = (P(None, "row", None, None, "col", None),)
    out_specs = P(None, "row", None, None, "col", None)
    return jax.shard_map(
        per_device, mesh=mesh, in_specs=in_specs, out_specs=out_specs, check_vma=False
    )
```

```python
import jax
import jax.numpy as jnp
from jax import lax
from jax.sharding import PartitionSpec as P

HIGH = lax.Precision.HIGHEST


def prescatter(pieces, axis, plan):
    me = lax.axis_index(axis)
    got = jnp.zeros_like(pieces[0])
    for q, pairs in enumerate(plan):
        moved = [(s, d) for s, d in pairs if s != d]
        kept = [s for s, d in pairs if s == d]
        if moved:
            got = got + lax.ppermute(pieces[q], axis, moved)
        for s in kept:
            got = got + jnp.where(me == s, pieces[q], jnp.zeros_like(pieces[q]))
    return got


def mm(a, b):
    return jnp.dot(a, b, precision=HIGH, preferred_element_type=jnp.float32)


def chol_and_inverse(a):
    a = (a + a.T) * 0.5
    h = a.shape[0] // 2
    eye = jnp.eye(h, dtype=a.dtype)
    l11 = jnp.tril(lax.linalg.cholesky(a[:h, :h], symmetrize_input=False))
    i11 = jax.scipy.linalg.solve_triangular(l11, eye, lower=True)
    l21 = mm(a[h:, :h], i11.T)
    s = a[h:, h:] - mm(l21, l21.T)
    s = (s + s.T) * 0.5
    l22 = jnp.tril(lax.linalg.cholesky(s, symmetrize_input=False))
    i22 = jax.scipy.linalg.solve_triangular(l22, eye, lower=True)
    i21 = -mm(i22, mm(l21, i11))
    zero = jnp.zeros((h, h), a.dtype)
    g = jnp.concatenate([jnp.concatenate([l11, zero], axis=1),
                         jnp.concatenate([l21, l22], axis=1)], axis=0)
    gi = jnp.concatenate([jnp.concatenate([i11, zero], axis=1),
                          jnp.concatenate([i21, i22], axis=1)], axis=0)
    return g, gi


def per_device(kernel):
    tiles, width, ucount = kernel.shape[0], kernel.shape[2], kernel.shape[3]
    work = kernel.reshape(tiles, width, ucount, width)
    nrow = lax.axis_size("row")
    ncol = lax.axis_size("col")
    my_row = lax.axis_index("row")
    my_col = lax.axis_index("col")
    half = width // 2

    rowblk = kernel[0, 0, :, :, 0, :]
    cpieces = [rowblk[(p % 2) * half:(p % 2 + 1) * half, p // 2, :] for p in range(2 * ucount)]
    d0 = [(-p) % nrow for p in range(2 * ucount)]
    d1 = [(1 + p) % nrow for p in range(2 * ucount)]
    cplan = [[(0, d0[p]), (1, d1[p])] for p in range(2 * ucount)]
    cmine = prescatter(cpieces, "row", cplan)
    cg = lax.all_gather(cmine, "row")

    def cblock(dest, u):
        return jnp.concatenate([cg[dest[2 * u]], cg[dest[2 * u + 1]]], axis=0)

    crow = [[cblock(d, u) for u in range(ucount)] for d in (d0, d1)]

    blk = kernel[0, 0, :, 0, 0, :]
    shifts = list(range(1, nrow))
    recv = jnp.stack([lax.ppermute(blk, "row", [(0, s), (1, (1 + s) % nrow)]) for s in shifts])
    from0 = lax.dynamic_index_in_dim(recv, jnp.maximum(my_row - 1, 0), keepdims=False)
    from1 = lax.dynamic_index_in_dim(recv, (my_row + nrow - 2) % nrow, keepdims=False)
    a0c = jnp.where(my_row == 0, blk, from0)
    a1c = jnp.where(my_row == 1, blk, from1)
    eye = jnp.eye(width, dtype=jnp.float32)
    pcol = kernel[:, 0, :, 0, 0, :].reshape(tiles * width, width)
    npieces = ncol // 2
    rrows = pcol.shape[0] // npieces
    rplan = [[(0, 2 * q), (1, 2 * q + 1)] for q in range(npieces)]
    rmine = prescatter([pcol[q * rrows:(q + 1) * rrows] for q in range(npieces)], "col", rplan)
    a0c, a1c, rmine = lax.optimization_barrier((a0c, a1c, rmine))
    swap = lax.ppermute(jnp.where(my_col == 0, a0c, a1c), "col", [(0, 1), (1, 0)])
    a00 = jnp.where(my_col == 0, a0c, swap)
    a11 = jnp.where(my_col == 0, swap, a1c)
    a10 = jnp.where(my_col == 0, a1c, a0c.T)
    g0, g0i = chol_and_inverse(a00)
    x01 = jnp.dot(a10, g0i.T, precision=HIGH, preferred_element_type=jnp.float32)
    a11u = a11 - jnp.dot(x01, x01.T, precision=HIGH, preferred_element_type=jnp.float32)
    g1, g1i = chol_and_inverse(a11u)
    res = jnp.concatenate([g0i, x01, g1i], axis=0)
    hres = res.shape[0] // 2
    lead = jnp.where(my_col == 0, res[:hres], res[hres:])
    lrows = lead.shape[0] // npieces
    lmine = prescatter([lead[q * lrows:(q + 1) * lrows] for q in range(npieces)], "col", rplan)
    rg = lax.all_gather(jnp.concatenate([rmine, lmine], axis=0), "col")
    rg = rg.reshape(npieces, 2, rrows + lrows, width)

    col0 = rg[:, 0, :rrows].reshape(tiles, width, width)
    col1 = rg[:, 1, :rrows].reshape(tiles, width, width)
    resg = jnp.concatenate([rg[:, 0, rrows:].reshape(hres, width),
                            rg[:, 1, rrows:].reshape(hres, width)], axis=0)
    g0i_all = resg[:width]
    x01_all = resg[width:2 * width]
    g1i_all = resg[2 * width:]

    block_rows = jnp.arange(tiles, dtype=jnp.int32) * nrow + my_row
    block_cols = jnp.arange(ucount, dtype=jnp.int32) * ncol + my_col
    cT0 = jnp.stack([crow[0][u].T for u in range(ucount)])
    cT1 = jnp.stack([crow[1][u].T for u in range(ucount)])

    def times_inv_t(y, ginv):
        return jnp.einsum("nab,cb->nac", y, ginv, precision=HIGH,
                          preferred_element_type=jnp.float32)

    x0 = times_inv_t(jnp.concatenate([col0, cT0], axis=0), g0i_all)
    x0r, x0c = x0[:tiles], x0[tiles:]
    y1 = jnp.concatenate([col1, cT1], axis=0) - times_inv_t(x0, x01_all)
    x1 = times_inv_t(y1, g1i_all)
    x1r, x1c = x1[:tiles], x1[tiles:]

    rows2d = tiles * width
    prod = jnp.dot(x0r.reshape(rows2d, width), x0c.reshape(ucount * width, width).T,
                   precision=HIGH, preferred_element_type=jnp.float32)
    prod = prod + jnp.dot(x1r.reshape(rows2d, width), x1c.reshape(ucount * width, width).T,
                          precision=HIGH, preferred_element_type=jnp.float32)
    whole = jnp.concatenate([kernel[:, 0, :, u, 0, :].reshape(rows2d, width) for u in range(ucount)],
                            axis=1)
    upd = whole - prod
    irow = block_rows[:, None, None]
    p0r = jnp.where(irow > 0, x0r, jnp.where(irow == 0, g0[None], 0.0))
    p1r = jnp.where(irow > 1, x1r, jnp.where(irow == 1, g1[None], 0.0))
    pan = jnp.where(my_col == 0, p0r, p1r).reshape(rows2d, width)
    top = jnp.repeat(block_rows < 2, width)[:, None]
    jcols = jnp.repeat(block_cols, width)[None, :]
    upd = jnp.where(top & (jcols >= 2), 0.0, upd)
    first = jnp.where(my_col < 2, pan, upd[:, :width])
    out = jnp.concatenate([first, upd[:, width:]], axis=1)
    return out.reshape(tiles, 1, width, ucount, 1, width)


def solution(mesh):
    in_specs = (P(None, "row", None, None, "col", None),)
    out_specs = P(None, "row", None, None, "col", None)
    return jax.shard_map(
        per_device, mesh=mesh, in_specs=in_specs, out_specs=out_specs, check_vma=False
    )
```
